1024 devices in a mesh: ctx: 128 (over z_lo, y, x), tp: 8 (over z_hi, core).
Axes of the slice: x: 4, y: 8, z: 16 (z_hi: 4, z_lo: 4; z = z_hi * 4 + z_lo), core: 2. Of those that a mesh axis runs over, the one named last changes fastest.
Arguments:
- projected: bfloat16 [3, 4096, 16384], P(None, 'tp', 'ctx'), may hold values from -6 to 6
- short_taps: bfloat16 [3, 7, 4096], P(None, None, 'tp'), may hold values from -2 to 2
- long_filter: float32 [4096, 16384], P(('tp', 'ctx')), may hold values from -1.1 to 1.1
- out_weight: bfloat16 [4096, 4096], P('tp'), may hold values from -0.09375 to 0.09375
- residual: bfloat16 [16384, 4096], P('ctx'), may hold values from -60 to 60
- norm_gain: float32 [4096], P('tp'), may hold values from 0.25 to 1.75
Outputs:
- residual_out: bfloat16 [16384, 4096], P('ctx', 'tp')
- normed_out: bfloat16 [16384, 4096], P('ctx', 'tp')
The draws below stay inside these ranges and needn't reach their ends.
All inputs are finite; a program needn't handle non-finite values.
Results may differ from the reference program's by a relative error of at most 0.014.
Values may be sent and summed in bfloat16 or wider, within the bound.
No kernel may reach another device: no remote copies, remote signals or barrier semaphores. Data moves between devices by JAX's collectives and lax.ppermute only.
A program may use at most 32 MiB of HBM per device.

```python
import jax
import jax.numpy as jnp
from jax import lax

MODEL_WIDTH = 4096
KF = 7
WINDOW_TOKENS = 16384
N_TP = 8


def draw_long_filter(key, part):
    random_keys = jax.random.split(key, 5)
    delay_index = jnp.arange(WINDOW_TOKENS, dtype=jnp.float32)[None, :]
    uniform_part = jax.random.uniform(random_keys[0], (MODEL_WIDTH, 1), jnp.float32)
    decay_len = jnp.exp(jnp.log(30.0) + uniform_part * jnp.log(100.0 * WINDOW_TOKENS / 30.0))
    rough = jnp.clip(jax.random.normal(random_keys[3], (MODEL_WIDTH, WINDOW_TOKENS), jnp.float32), -4.0, 4.0)
    spike_position = jax.random.randint(random_keys[4], (MODEL_WIDTH, 3), 0, WINDOW_TOKENS).astype(jnp.float32)
    multiplier = jnp.ones((MODEL_WIDTH, WINDOW_TOKENS), jnp.float32)
    for spike_index in range(3):
        multiplier = multiplier * jnp.where(delay_index >= spike_position[:, spike_index:spike_index + 1], 0.6, 1.0)
    amplitude = jnp.sqrt(1.0 - jnp.exp(-2.0 / decay_len))
    return amplitude * jnp.exp(-delay_index / decay_len) * rough * multiplier


def draw_residual(key, part):
    random_keys = jax.random.split(key, 3)
    column_rise = jnp.exp(jnp.log(3.0) * jnp.arange(MODEL_WIDTH, dtype=jnp.float32) / MODEL_WIDTH)[None, :]
    column_scale = jnp.exp(jax.random.uniform(random_keys[0], (1, MODEL_WIDTH), jnp.float32) * jnp.log(10.0)) * column_rise
    row_scale = jnp.exp(jax.random.uniform(random_keys[1], (WINDOW_TOKENS, 1), jnp.float32) * jnp.log(10.0))
    values = jnp.clip(jax.random.normal(random_keys[2], (WINDOW_TOKENS, MODEL_WIDTH), jnp.float32), -4.0, 4.0)
    return (0.05 * row_scale * column_scale * values).astype(jnp.bfloat16)


def steps_of(rng, dims, shards, least, high):
    level = 1.0
    for position, blocks in shards:
        draws = jax.random.uniform(jax.random.fold_in(jax.random.fold_in(rng, 6), position), (blocks,), jnp.float32, least / len(shards), high / len(shards))
        level = level * jnp.repeat(jnp.exp(draws), dims[position] // blocks).reshape((-1,) + (1,) * (len(dims) - 1 - position))
    return level


def centred(stream_key, extent, deviation, reach, cuts=(), kind=jnp.bfloat16):
    result = deviation * jax.random.normal(stream_key, extent, jnp.float32)
    if cuts:
        result = result * steps_of(stream_key, extent, cuts, -0.22, 0.18)
    return jnp.clip(result, -reach, reach).astype(kind)


def setup_inputs(seed: int = 0) -> dict:
    seeds = jax.random.split(jax.random.key(seed), 7)
    projected = centred(seeds[0], (3, MODEL_WIDTH, WINDOW_TOKENS), 1.0, 6.0, ((1, 8), (2, 128)))
    short_taps = centred(seeds[1], (3, KF, MODEL_WIDTH), KF ** -0.5, 2.0, ((2, 8),))
    long_filter = draw_long_filter(jax.random.fold_in(seeds[6], 71), 0)
    out_weight = centred(seeds[3], (MODEL_WIDTH, MODEL_WIDTH), MODEL_WIDTH ** -0.5, 0.09375, ((0, 8),))
    residual = draw_residual(jax.random.fold_in(seeds[6], 71), 0)
    norm_gain = jnp.clip(1.0 + 0.15 * jax.random.normal(seeds[5], (MODEL_WIDTH,), jnp.float32), 0.25, 1.75)
    return dict(projected=projected, short_taps=short_taps, long_filter=long_filter, out_weight=out_weight, residual=residual, norm_gain=norm_gain)


epsilon = 1e-06

def mix_block(pieces):
    streams, tap_block, filter_block = pieces
    length = streams.shape[2]
    tap_count = tap_block.shape[1]
    padded = jnp.pad(streams.astype(jnp.float32), ((0, 0), (0, 0), (tap_count - 1, 0)))
    shaped = jnp.zeros(streams.shape, jnp.float32)
    for tap_index in range(tap_count):
        shaped = shaped + tap_block[:, tap_index, :].astype(jnp.float32)[:, :, None] * padded[:, :, tap_index:tap_index + length]
    product = (shaped[1] * shaped[2]).astype(jnp.bfloat16)
    fft_size = 2 * length
    spectrum = jnp.fft.rfft(product.astype(jnp.float32), n=fft_size, axis=1) * jnp.fft.rfft(filter_block, n=fft_size, axis=1)
    conv = jnp.fft.irfft(spectrum, n=fft_size, axis=1)[:, :length].astype(jnp.bfloat16)
    return (shaped[0] * conv.astype(jnp.float32)).astype(jnp.bfloat16)

def reference(projected, short_taps, long_filter, out_weight, residual, norm_gain):
    channels = projected.shape[1]
    length = projected.shape[2]
    block_ch = min(256, channels)
    block_count = channels // block_ch
    stream_blocks = projected.reshape(3, block_count, block_ch, length).transpose(1, 0, 2, 3)
    tap_blocks = short_taps.reshape(3, short_taps.shape[1], block_count, block_ch).transpose(2, 0, 1, 3)
    filter_blocks = long_filter.reshape(block_count, block_ch, length)
    gated = lax.map(mix_block, (stream_blocks, tap_blocks, filter_blocks)).reshape(channels, length)
    group_ch = channels // N_TP
    projection = jnp.zeros((length, channels), jnp.float32)
    for group_index in range(N_TP):
        rows_lo = group_index * group_ch
        partial_value = jnp.dot(gated[rows_lo:rows_lo + group_ch].T, out_weight[rows_lo:rows_lo + group_ch], preferred_element_type=jnp.float32)
        partial_value = lax.optimization_barrier(partial_value.astype(jnp.bfloat16))
        projection = projection + partial_value.astype(jnp.float32)
    summed = residual.astype(jnp.float32) + projection
    residual_out = summed.astype(jnp.bfloat16)
    inverse_rms = lax.rsqrt(lax.optimization_barrier(jnp.mean(summed * summed, axis=1, keepdims=True)) + epsilon)
    normed_out = (summed * inverse_rms * norm_gain.astype(jnp.float32)[None, :]).astype(jnp.bfloat16)
    return (residual_out, normed_out)
```

```python
import math

import jax
import jax.numpy as jnp
from jax import lax
from jax.sharding import Mesh, PartitionSpec as P

epsilon = 1e-06
REDUCE_MODE = "flat"
TP_AXES = "tp"
highest = lax.Precision.HIGHEST


def passed_along(block, axis, distance):
    devices = range(lax.axis_size(axis))
    route = [(i - distance, i) for i in devices if i - distance in devices]
    return lax.ppermute(block, axis, route)


def angle_table(row_count, col_count, period):
    row_index = lax.iota(jnp.int32, row_count)[:, None]
    col_index = lax.iota(jnp.int32, col_count)[None, :]
    phase_int = row_index * col_index % period
    angles = phase_int.astype(jnp.float32) * (2.0 * math.pi / period)
    return (jnp.cos(angles), jnp.sin(angles))


def contract(form, first_arg, second_arg):
    return jnp.einsum(form, first_arg, second_arg, precision=highest)


def forward_dft(signal, tables):
    first_cos, first_sin, twist_cos, twist_sin, inner_cos, inner_sin = tables
    real_one = contract("cma,mk->cka", signal, first_cos)
    imag_one = -contract("cma,mk->cka", signal, first_sin)
    real_two = real_one * twist_cos + imag_one * twist_sin
    imag_two = imag_one * twist_cos - real_one * twist_sin
    real_out = contract("cka,aj->ckj", real_two, inner_cos) + contract(
        "cka,aj->ckj", imag_two, inner_sin
    )
    imag_out = contract("cka,aj->ckj", imag_two, inner_cos) - contract(
        "cka,aj->ckj", real_two, inner_sin
    )
    return (real_out, imag_out)


def inverse_dft(real_in, imag_in, tables, length_total):
    first_cos, first_sin, twist_cos, twist_sin, inner_cos, inner_sin = tables
    real_one = contract("ckj,ja->cka", real_in, inner_cos) - contract(
        "ckj,ja->cka", imag_in, inner_sin
    )
    imag_one = contract("ckj,ja->cka", imag_in, inner_cos) + contract(
        "ckj,ja->cka", real_in, inner_sin
    )
    real_two = real_one * twist_cos - imag_one * twist_sin
    imag_two = imag_one * twist_cos + real_one * twist_sin
    signal = contract("mk,cka->cma", first_cos, real_two) - contract(
        "mk,cka->cma", first_sin, imag_two
    )
    return signal / length_total


def body(projected, short_taps, long_filter, out_weight, residual, norm_gain):
    tap_count = short_taps.shape[1]
    tok_rows = projected.shape[2]
    rim_rows = passed_along(projected[:, :, tok_rows - (tap_count - 1) :], "ctx", 1)
    extended = jnp.concatenate([rim_rows, projected], axis=2)
    shaped = jnp.zeros(projected.shape, jnp.float32)
    for tap_index in range(tap_count):
        window_rows = extended[:, :, tap_index : tap_index + tok_rows].astype(jnp.float32)
        shaped = shaped + short_taps[:, tap_index, :].astype(jnp.float32)[:, :, None] * window_rows
    product = (shaped[1] * shaped[2]).astype(jnp.bfloat16)
    spread = lax.all_to_all(product, "ctx", split_axis=0, concat_axis=1, tiled=True)
    ctx_count = lax.axis_size("ctx")
    full_m = 2 * ctx_count
    length_total = tok_rows * full_m
    first_cos, first_sin = angle_table(ctx_count, full_m, full_m)
    twist_cos, twist_sin = angle_table(full_m, tok_rows, length_total)
    inner_cos, inner_sin = angle_table(tok_rows, tok_rows, tok_rows)
    tables = (first_cos, first_sin, twist_cos, twist_sin, inner_cos, inner_sin)
    conv_ch = spread.shape[0]
    signal = spread.astype(jnp.float32).reshape(conv_ch, ctx_count, tok_rows)
    filter_rows = long_filter.reshape(conv_ch, ctx_count, tok_rows)
    signal_real, signal_imag = forward_dft(signal, tables)
    filter_real, filter_imag = forward_dft(filter_rows, tables)
    spectrum_real = signal_real * filter_real - signal_imag * filter_imag
    spectrum_imag = signal_real * filter_imag + signal_imag * filter_real
    filtered = inverse_dft(spectrum_real, spectrum_imag, tables, length_total)
    conv = filtered.reshape(conv_ch, ctx_count * tok_rows).astype(jnp.bfloat16)
    returned = lax.all_to_all(conv, "ctx", split_axis=1, concat_axis=0, tiled=True)
    gated = (shaped[0] * returned.astype(jnp.float32)).astype(jnp.bfloat16)
    partial_value = lax.dot_general(
        gated, out_weight, (((0,), (0,)), ((), ())), preferred_element_type=jnp.float32
    )
    tok_count, col_count = partial_value.shape
    group_ch = out_weight.shape[0]
    if REDUCE_MODE == "flat":
        own_part = lax.psum_scatter(
            partial_value.astype(jnp.bfloat16), TP_AXES, scatter_dimension=1, tiled=True
        )
    else:
        zh_count = lax.axis_size("zh")
        co_count = lax.axis_size("co")
        blocks = partial_value.astype(jnp.bfloat16).reshape(tok_count, zh_count, co_count, group_ch)
        blocks = blocks.transpose(0, 2, 1, 3).reshape(tok_count, col_count)
        half_part = lax.psum_scatter(blocks, "co", scatter_dimension=1, tiled=True)
        own_part = lax.psum_scatter(half_part, "zh", scatter_dimension=1, tiled=True)
    start_col = lax.axis_index(TP_AXES) * group_ch
    own_res = lax.dynamic_slice_in_dim(residual, start_col, group_ch, 1)
    own_rows = own_res.astype(jnp.float32) + own_part.astype(jnp.float32)
    square_sum = lax.psum(jnp.sum(own_rows * own_rows, axis=1), TP_AXES)
    inverse_rms = lax.rsqrt(square_sum / col_count + epsilon)
    residual_out = own_rows.astype(jnp.bfloat16)
    normed_out = (own_rows * inverse_rms[:, None] * norm_gain[None, :]).astype(jnp.bfloat16)
    return (residual_out, normed_out)


def solution(mesh):
    tp_spec = TP_AXES
    placed = (
        P(None, tp_spec, "ctx"),
        P(None, None, tp_spec),
        P((tp_spec, "ctx") if isinstance(tp_spec, str) else (*tp_spec, "ctx"), None),
        P(tp_spec, None),
        P("ctx", None),
        P(tp_spec),
    )
    if isinstance(tp_spec, str):
        run_mesh = mesh
    else:
        ctx_count, tp_count = mesh.devices.shape
        run_mesh = Mesh(mesh.devices.reshape(ctx_count, tp_count // 2, 2), ("ctx", "zh", "co"))
    return jax.shard_map(
        body,
        mesh=run_mesh,
        in_specs=placed,
        out_specs=(P("ctx", tp_spec), P("ctx", tp_spec)),
        check_vma=False,
    )
```

```python
import math

import jax
import jax.numpy as jnp
from jax import lax
from jax.sharding import Mesh, PartitionSpec as P

epsilon = 1e-06
SCATTER_MODE = "a2a_zh"
TOTAL_MODE = "gather"
TP_AXES = ("zh", "co")
highest = lax.Precision.HIGHEST


def passed_along(block, axis, distance):
    devices = range(lax.axis_size(axis))
    route = [(i - distance, i) for i in devices if i - distance in devices]
    return lax.ppermute(block, axis, route)


def angle_table(row_count, col_count, period):
    row_index = lax.iota(jnp.int32, row_count)[:, None]
    col_index = lax.iota(jnp.int32, col_count)[None, :]
    phase_int = row_index * col_index % period
    angles = phase_int.astype(jnp.float32) * (2.0 * math.pi / period)
    return (jnp.cos(angles), jnp.sin(angles))


def contract(form, first_arg, second_arg):
    return jnp.einsum(form, first_arg, second_arg, precision=highest)


def forward_dft(signal, tables):
    first_cos, first_sin, twist_cos, twist_sin, inner_cos, inner_sin = tables
    real_one = contract("cma,mk->cka", signal, first_cos)
    imag_one = -contract("cma,mk->cka", signal, first_sin)
    real_two = real_one * twist_cos + imag_one * twist_sin
    imag_two = imag_one * twist_cos - real_one * twist_sin
    real_out = contract("cka,aj->ckj", real_two, inner_cos) + contract(
        "cka,aj->ckj", imag_two, inner_sin
    )
    imag_out = contract("cka,aj->ckj", imag_two, inner_cos) - contract(
        "cka,aj->ckj", real_two, inner_sin
    )
    return (real_out, imag_out)


def inverse_dft(real_in, imag_in, tables, length_total):
    first_cos, first_sin, twist_cos, twist_sin, inner_cos, inner_sin = tables
    real_one = contract("ckj,ja->cka", real_in, inner_cos) - contract(
        "ckj,ja->cka", imag_in, inner_sin
    )
    imag_one = contract("ckj,ja->cka", imag_in, inner_cos) + contract(
        "ckj,ja->cka", real_in, inner_sin
    )
    real_two = real_one * twist_cos - imag_one * twist_sin
    imag_two = imag_one * twist_cos + real_one * twist_sin
    signal = contract("mk,cka->cma", first_cos, real_two) - contract(
        "mk,cka->cma", first_sin, imag_two
    )
    return signal / length_total


def swapped(block, axis, distance):
    count = lax.axis_size(axis)
    route = [(i, (i + distance) % count) for i in range(count)]
    return lax.ppermute(block, axis, route)


def ring_scatter(partial_value, group_ch):
    tok_count = partial_value.shape[0]
    zh_count = lax.axis_size("zh")
    zh_index = lax.axis_index("zh")
    co_index = lax.axis_index("co")
    blocks = partial_value.reshape(tok_count, zh_count, 2, group_ch)
    mine = lax.dynamic_index_in_dim(blocks, co_index, 2, keepdims=False)
    other = lax.dynamic_index_in_dim(blocks, 1 - co_index, 2, keepdims=False)
    acc = mine + swapped(other.astype(jnp.bfloat16), "co", 1).astype(jnp.float32)
    if SCATTER_MODE == "a2a_tp":
        order = blocks.transpose(1, 2, 0, 3).astype(jnp.bfloat16)
        got = lax.all_to_all(order.reshape(zh_count * 2, tok_count, group_ch), TP_AXES, 0, 0, tiled=True)
        return jnp.sum(got.astype(jnp.float32), axis=0)
    if SCATTER_MODE == "a2a_zh":
        order = acc.transpose(1, 0, 2).astype(jnp.bfloat16)
        got = lax.all_to_all(order, "zh", 0, 0, tiled=True)
        return mine_total(got, acc, zh_index)
    if SCATTER_MODE == "direct":
        total = lax.dynamic_index_in_dim(acc, zh_index, 1, keepdims=False)
        for distance in range(1, zh_count):
            chunk = lax.dynamic_index_in_dim(acc, (zh_index + distance) % zh_count, 1, keepdims=False)
            total = total + swapped(chunk.astype(jnp.bfloat16), "zh", distance).astype(jnp.float32)
        return total
    half = group_ch // 2
    ahead = acc[:, :, :half]
    behind = acc[:, :, half:]
    send_a = lax.dynamic_index_in_dim(ahead, (zh_index - 1) % zh_count, 1, keepdims=False)
    send_b = lax.dynamic_index_in_dim(behind, (zh_index + 1) % zh_count, 1, keepdims=False)
    for step in range(zh_count - 1):
        got_a = swapped(send_a.astype(jnp.bfloat16), "zh", 1).astype(jnp.float32)
        got_b = swapped(send_b.astype(jnp.bfloat16), "zh", zh_count - 1).astype(jnp.float32)
        send_a = got_a + lax.dynamic_index_in_dim(ahead, (zh_index - step - 2) % zh_count, 1, keepdims=False)
        send_b = got_b + lax.dynamic_index_in_dim(behind, (zh_index + step + 2) % zh_count, 1, keepdims=False)
    return jnp.concatenate([send_a, send_b], axis=1)


def mine_total(got, acc, zh_index):
    own = lax.dynamic_index_in_dim(acc, zh_index, 1, keepdims=False)
    count = got.shape[0]
    total = own
    for source in range(count):
        keep = jnp.where(source == zh_index, 0.0, 1.0).astype(jnp.float32)
        total = total + keep * got[source].astype(jnp.float32)
    return total


def row_total(values):
    if TOTAL_MODE == "psum":
        return lax.psum(values, TP_AXES)
    if TOTAL_MODE == "gather":
        return jnp.sum(lax.all_gather(values, TP_AXES, axis=0, tiled=False), axis=0)
    total = values + swapped(values, "co", 1)
    zh_count = lax.axis_size("zh")
    step = 1
    while step < zh_count:
        route = [(i, i ^ step) for i in range(zh_count)]
        total = total + lax.ppermute(total, "zh", route)
        step *= 2
    return total


def body(projected, short_taps, long_filter, out_weight, residual, norm_gain):
    tap_count = short_taps.shape[1]
    tok_rows = projected.shape[2]
    rim_rows = passed_along(projected[:, :, tok_rows - (tap_count - 1) :], "ctx", 1)
    extended = jnp.concatenate([rim_rows, projected], axis=2)
    shaped = jnp.zeros(projected.shape, jnp.float32)
    for tap_index in range(tap_count):
        window_rows = extended[:, :, tap_index : tap_index + tok_rows].astype(jnp.float32)
        shaped = shaped + short_taps[:, tap_index, :].astype(jnp.float32)[:, :, None] * window_rows
    product = (shaped[1] * shaped[2]).astype(jnp.bfloat16)
    spread = lax.all_to_all(product, "ctx", split_axis=0, concat_axis=1, tiled=True)
    ctx_count = lax.axis_size("ctx")
    full_m = 2 * ctx_count
    length_total = tok_rows * full_m
    first_cos, first_sin = angle_table(ctx_count, full_m, full_m)
    twist_cos, twist_sin = angle_table(full_m, tok_rows, length_total)
    inner_cos, inner_sin = angle_table(tok_rows, tok_rows, tok_rows)
    tables = (first_cos, first_sin, twist_cos, twist_sin, inner_cos, inner_sin)
    conv_ch = spread.shape[0]
    signal = spread.astype(jnp.float32).reshape(conv_ch, ctx_count, tok_rows)
    filter_rows = long_filter.reshape(conv_ch, ctx_count, tok_rows)
    signal_real, signal_imag = forward_dft(signal, tables)
    filter_real, filter_imag = forward_dft(filter_rows, tables)
    spectrum_real = signal_real * filter_real - signal_imag * filter_imag
    spectrum_imag = signal_real * filter_imag + signal_imag * filter_real
    filtered = inverse_dft(spectrum_real, spectrum_imag, tables, length_total)
    conv = filtered.reshape(conv_ch, ctx_count * tok_rows).astype(jnp.bfloat16)
    returned = lax.all_to_all(conv, "ctx", split_axis=1, concat_axis=0, tiled=True)
    gated = (shaped[0] * returned.astype(jnp.float32)).astype(jnp.bfloat16)
    partial_value = lax.dot_general(
        gated, out_weight, (((0,), (0,)), ((), ())), preferred_element_type=jnp.float32
    )
    tok_count, col_count = partial_value.shape
    group_ch = out_weight.shape[0]
    own_part = ring_scatter(partial_value, group_ch)
    start_col = lax.axis_index(TP_AXES) * group_ch
    own_res = lax.dynamic_slice_in_dim(residual, start_col, group_ch, 1)
    own_rows = own_res.astype(jnp.float32) + own_part.astype(jnp.float32)
    square_sum = row_total(jnp.sum(own_rows * own_rows, axis=1))
    inverse_rms = lax.rsqrt(square_sum / col_count + epsilon)
    residual_out = own_rows.astype(jnp.bfloat16)
    normed_out = (own_rows * inverse_rms[:, None] * norm_gain[None, :]).astype(jnp.bfloat16)
    return (residual_out, normed_out)


def solution(mesh):
    tp_spec = TP_AXES
    placed = (
        P(None, tp_spec, "ctx"),
        P(None, None, tp_spec),
        P((tp_spec, "ctx") if isinstance(tp_spec, str) else (*tp_spec, "ctx"), None),
        P(tp_spec, None),
        P("ctx", None),
        P(tp_spec),
    )
    if isinstance(tp_spec, str):
        run_mesh = mesh
    else:
        ctx_count, tp_count = mesh.devices.shape
        run_mesh = Mesh(mesh.devices.reshape(ctx_count, tp_count // 2, 2), ("ctx", "zh", "co"))
    return jax.shard_map(
        body,
        mesh=run_mesh,
        in_specs=placed,
        out_specs=(P("ctx", tp_spec), P("ctx", tp_spec)),
        check_vma=False,
    )
```

```python
import math

import jax
import jax.numpy as jnp
from jax import lax
from jax.sharding import Mesh, PartitionSpec as P

epsilon = 1e-06
SCATTER_MODE = "a2a_zh"
TOTAL_MODE = "gather"
TP_AXES = ("zh", "co")
highest = lax.Precision.HIGHEST


def passed_along(block, axis, distance):
    devices = range(lax.axis_size(axis))
    route = [(i - distance, i) for i in devices if i - distance in devices]
    return lax.ppermute(block, axis, route)


def angle_table(row_count, col_count, period):
    row_index = lax.iota(jnp.int32, row_count)[:, None]
    col_index = lax.iota(jnp.int32, col_count)[None, :]
    phase_int = row_index * col_index % period
    angles = phase_int.astype(jnp.float32) * (2.0 * math.pi / period)
    return (jnp.cos(angles), jnp.sin(angles))


def contract(form, first_arg, second_arg):
    return jnp.einsum(form, first_arg, second_arg, precision=highest)


def forward_dft(signal, tables):
    first_cos, first_sin, twist_cos, twist_sin, inner_cos, inner_sin = tables
    real_one = contract("cma,mk->cka", signal, first_cos)
    imag_one = -contract("cma,mk->cka", signal, first_sin)
    real_two = real_one * twist_cos + imag_one * twist_sin
    imag_two = imag_one * twist_cos - real_one * twist_sin
    real_out = contract("cka,aj->ckj", real_two, inner_cos) + contract(
        "cka,aj->ckj", imag_two, inner_sin
    )
    imag_out = contract("cka,aj->ckj", imag_two, inner_cos) - contract(
        "cka,aj->ckj", real_two, inner_sin
    )
    return (real_out, imag_out)


def inverse_dft(real_in, imag_in, tables, length_total):
    first_cos, first_sin, twist_cos, twist_sin, inner_cos, inner_sin = tables
    real_one = contract("ckj,ja->cka", real_in, inner_cos) - contract(
        "ckj,ja->cka", imag_in, inner_sin
    )
    imag_one = contract("ckj,ja->cka", imag_in, inner_cos) + contract(
        "ckj,ja->cka", real_in, inner_sin
    )
    real_two = real_one * twist_cos - imag_one * twist_sin
    imag_two = imag_one * twist_cos + real_one * twist_sin
    signal = contract("mk,cka->cma", first_cos, real_two) - contract(
        "mk,cka->cma", first_sin, imag_two
    )
    return signal / length_total


def swapped(block, axis, distance):
    count = lax.axis_size(axis)
    route = [(i, (i + distance) % count) for i in range(count)]
    return lax.ppermute(block, axis, route)


def ring_scatter(partial_value, group_ch):
    tok_count = partial_value.shape[0]
    zh_count = lax.axis_size("zh")
    zh_index = lax.axis_index("zh")
    co_index = lax.axis_index("co")
    blocks = partial_value.reshape(tok_count, zh_count, 2, group_ch)
    mine = lax.dynamic_index_in_dim(blocks, co_index, 2, keepdims=False)
    other = lax.dynamic_index_in_dim(blocks, 1 - co_index, 2, keepdims=False)
    acc = mine + swapped(other.astype(jnp.bfloat16), "co", 1).astype(jnp.float32)
    if SCATTER_MODE == "a2a_tp":
        order = blocks.transpose(1, 2, 0, 3).astype(jnp.bfloat16)
        got = lax.all_to_all(order.reshape(zh_count * 2, tok_count, group_ch), TP_AXES, 0, 0, tiled=True)
        return jnp.sum(got.astype(jnp.float32), axis=0)
    if SCATTER_MODE == "a2a_zh":
        order = acc.transpose(1, 0, 2).astype(jnp.bfloat16)
        got = lax.all_to_all(order, "zh", 0, 0, tiled=True)
        return mine_total(got, acc, zh_index)
    if SCATTER_MODE == "direct":
        total = lax.dynamic_index_in_dim(acc, zh_index, 1, keepdims=False)
        for distance in range(1, zh_count):
            chunk = lax.dynamic_index_in_dim(acc, (zh_index + distance) % zh_count, 1, keepdims=False)
            total = total + swapped(chunk.astype(jnp.bfloat16), "zh", distance).astype(jnp.float32)
        return total
    half = group_ch // 2
    ahead = acc[:, :, :half]
    behind = acc[:, :, half:]
    send_a = lax.dynamic_index_in_dim(ahead, (zh_index - 1) % zh_count, 1, keepdims=False)
    send_b = lax.dynamic_index_in_dim(behind, (zh_index + 1) % zh_count, 1, keepdims=False)
    for step in range(zh_count - 1):
        got_a = swapped(send_a.astype(jnp.bfloat16), "zh", 1).astype(jnp.float32)
        got_b = swapped(send_b.astype(jnp.bfloat16), "zh", zh_count - 1).astype(jnp.float32)
        send_a = got_a + lax.dynamic_index_in_dim(ahead, (zh_index - step - 2) % zh_count, 1, keepdims=False)
        send_b = got_b + lax.dynamic_index_in_dim(behind, (zh_index + step + 2) % zh_count, 1, keepdims=False)
    return jnp.concatenate([send_a, send_b], axis=1)


def mine_total(got, acc, zh_index):
    own = lax.dynamic_index_in_dim(acc, zh_index, 1, keepdims=False)
    count = got.shape[0]
    total = own
    for source in range(count):
        keep = jnp.where(source == zh_index, 0.0, 1.0).astype(jnp.float32)
        total = total + keep * got[source].astype(jnp.float32)
    return total


def row_total(values):
    if TOTAL_MODE == "psum":
        return lax.psum(values, TP_AXES)
    if TOTAL_MODE == "gather":
        return jnp.sum(lax.all_gather(values, TP_AXES, axis=0, tiled=False), axis=0)
    total = values + swapped(values, "co", 1)
    zh_count = lax.axis_size("zh")
    step = 1
    while step < zh_count:
        route = [(i, i ^ step) for i in range(zh_count)]
        total = total + lax.ppermute(total, "zh", route)
        step *= 2
    return total


def body(projected, short_taps, long_filter, out_weight, residual, norm_gain):
    tap_count = short_taps.shape[1]
    tok_rows = projected.shape[2]
    rim_rows = passed_along(projected[:, :, tok_rows - (tap_count - 1) :], "ctx", 1)
    extended = jnp.concatenate([rim_rows, projected], axis=2)
    shaped = jnp.zeros(projected.shape, jnp.float32)
    for tap_index in range(tap_count):
        window_rows = extended[:, :, tap_index : tap_index + tok_rows].astype(jnp.float32)
        shaped = shaped + short_taps[:, tap_index, :].astype(jnp.float32)[:, :, None] * window_rows
    product = (shaped[1] * shaped[2]).astype(jnp.bfloat16)
    spread = lax.all_to_all(product, "ctx", split_axis=0, concat_axis=1, tiled=True)
    ctx_count = lax.axis_size("ctx")
    full_m = 2 * ctx_count
    length_total = tok_rows * full_m
    first_cos, first_sin = angle_table(ctx_count, full_m, full_m)
    twist_cos, twist_sin = angle_table(full_m, tok_rows, length_total)
    inner_cos, inner_sin = angle_table(tok_rows, tok_rows, tok_rows)
    tables = (first_cos, first_sin, twist_cos, twist_sin, inner_cos, inner_sin)
    conv_ch = spread.shape[0]
    signal = spread.astype(jnp.float32).reshape(conv_ch, ctx_count, tok_rows)
    filter_rows = long_filter.reshape(conv_ch, ctx_count, tok_rows)
    signal_real, signal_imag = forward_dft(signal, tables)
    filter_real, filter_imag = forward_dft(filter_rows, tables)
    spectrum_real = signal_real * filter_real - signal_imag * filter_imag
    spectrum_imag = signal_real * filter_imag + signal_imag * filter_real
    filtered = inverse_dft(spectrum_real, spectrum_imag, tables, length_total)
    conv = filtered.reshape(conv_ch, ctx_count * tok_rows).astype(jnp.bfloat16)
    returned = lax.all_to_all(conv, "ctx", split_axis=1, concat_axis=0, tiled=True)
    gated = (shaped[0] * returned.astype(jnp.float32)).astype(jnp.bfloat16)
    partial_value = lax.dot_general(
        gated, out_weight, (((0,), (0,)), ((), ())), preferred_element_type=jnp.float32
    )
    tok_count, col_count = partial_value.shape
    group_ch = out_weight.shape[0]
    half_cols = group_ch // 2
    weight_blocks = out_weight.reshape(group_ch, col_count // group_ch, group_ch)
    pieces = []
    for piece in range(2):
        weight_piece = weight_blocks[:, :, piece * half_cols : (piece + 1) * half_cols]
        piece_value = lax.dot_general(
            gated, weight_piece.reshape(group_ch, -1), (((0,), (0,)), ((), ())),
            preferred_element_type=jnp.float32,
        )
        pieces.append(ring_scatter(piece_value, half_cols))
    own_part = jnp.concatenate(pieces, axis=1)
    start_col = lax.axis_index(TP_AXES) * group_ch
    own_res = lax.dynamic_slice_in_dim(residual, start_col, group_ch, 1)
    own_rows = own_res.astype(jnp.float32) + own_part.astype(jnp.float32)
    square_sum = row_total(jnp.sum(own_rows * own_rows, axis=1))
    inverse_rms = lax.rsqrt(square_sum / col_count + epsilon)
    residual_out = own_rows.astype(jnp.bfloat16)
    normed_out = (own_rows * inverse_rms[:, None] * norm_gain[None, :]).astype(jnp.bfloat16)
    return (residual_out, normed_out)


def solution(mesh):
    tp_spec = TP_AXES
    placed = (
        P(None, tp_spec, "ctx"),
        P(None, None, tp_spec),
        P((tp_spec, "ctx") if isinstance(tp_spec, str) else (*tp_spec, "ctx"), None),
        P(tp_spec, None),
        P("ctx", None),
        P(tp_spec),
    )
    if isinstance(tp_spec, str):
        run_mesh = mesh
    else:
        ctx_count, tp_count = mesh.devices.shape
        run_mesh = Mesh(mesh.devices.reshape(ctx_count, tp_count // 2, 2), ("ctx", "zh", "co"))
    return jax.shard_map(
        body,
        mesh=run_mesh,
        in_specs=placed,
        out_specs=(P("ctx", tp_spec), P("ctx", tp_spec)),
        check_vma=False,
    )
```
